512 devices in a mesh: tile: 128 (over x, z, core), epoch: 4 (over y).
Axes of the slice: x: 4, y: 4, z: 16, core: 2. Of those that a mesh axis runs over, the one named last changes fastest.
Arguments:
- psi: float32 [48, 4096, 512], P('epoch', 'tile'), may hold values from -6 to 6
- phi: float32 [48, 4096, 512], P('epoch', 'tile'), may hold values from 0.5 to 4
- shifts: int32 [8, 48, 2], replicated, may hold values from -16 to 16, as said below
Outputs:
- best_likelihood: float32 [4096, 512], P('tile', 'epoch')
The draws below stay inside these ranges and needn't reach their ends.
Inputs may be any that keep to these rules, and one draw needn't show every extreme that they name: shifts[v, e, :] = floor(r_v * t_e / 64) for integer rates r_v of -16 to 16 per component and integer times t_e of 0 to 64; the first epoch has time 0 and the last 64; both extremes are reached.
All inputs are finite; a program needn't handle non-finite values.
Results may differ from the reference program's by a relative error of at most 0.0003.
Values sent between devices are 32-bit elements; how exact they have to be, the bound alone decides.
No kernel may reach another device: no remote copies, remote signals or barrier semaphores. Data moves between devices by JAX's collectives and lax.ppermute only.
A program may use at most 64 MiB of HBM per device.

```python
import math
import jax
import jax.numpy as jnp
from jax import lax

W = 512
VELS = 8
HALO = 16
TSPAN = 64
EPOCHS = 48
ROWS = 4096


def draw_shifts(key, part):
    key_time = jax.random.fold_in(key, 11)
    key_rate = jax.random.fold_in(key, 12)
    times = jax.random.randint(key_time, (EPOCHS,), 0, TSPAN + 1)
    times = times.at[0].set(0).at[EPOCHS - 1].set(TSPAN)
    rates = jax.random.randint(key_rate, (VELS, 2), -HALO, HALO + 1)
    rates = rates.at[0].set(jnp.array([HALO, HALO], jnp.int32))
    rates = rates.at[1].set(jnp.array([-HALO, -HALO], jnp.int32))
    return (rates[:, None, :] * times[None, :, None] // TSPAN).astype(jnp.int32)


def levels(own_key, extent, split, least, high):
    factor_of, own = 1.0, jax.random.fold_in(own_key, 6)
    for axis_at, blocks in split:
        draws = jnp.exp(jax.random.uniform(jax.random.fold_in(own, axis_at), (blocks,), jnp.float32, least / len(split), high / len(split)))
        factor_of = factor_of * jnp.repeat(draws, extent[axis_at] // blocks).reshape([-1 if axis == axis_at else 1 for axis in range(len(extent))])
    return factor_of


def bell_draw(rng, extent, width, bound, pieces=(), dtype=jnp.bfloat16):
    factor_of = levels(rng, extent, pieces, -0.22, 0.18) if pieces else 1.0
    entries = jax.random.normal(rng, extent, jnp.float32) * width * factor_of
    return jnp.minimum(jnp.maximum(entries, -bound), bound).astype(dtype)


def setup_inputs(seed: int = 0) -> dict:
    key_list = jax.random.split(jax.random.key(seed), 4)
    psi = bell_draw(key_list[0], (EPOCHS, ROWS, W), 1.0, 6.0, ((0, 4), (1, 128)), jnp.float32)
    phi = jnp.clip(jnp.exp(math.log(4.0) - 2.0794415 * jax.random.uniform(key_list[1], (EPOCHS, ROWS, W), jnp.float32) ** levels(key_list[1], (EPOCHS, ROWS, W), ((0, 4), (1, 128)), -0.2, 0.2)), 0.5, 4.0)
    shifts = draw_shifts(jax.random.fold_in(key_list[3], 71), 0)
    return dict(psi=psi, phi=phi, shifts=shifts)


def reference(psi, phi, shifts):
    stacked = jnp.stack([psi, phi])
    padded = jnp.pad(stacked, ((0, 0), (0, 0), (HALO, HALO), (HALO, HALO)))
    zero = jnp.zeros((), jnp.int32)

    def one_velocity(offsets):

        def add(e, total):
            rows = (HALO + offsets[e, 0]).astype(jnp.int32)
            cols = (HALO + offsets[e, 1]).astype(jnp.int32)
            piece = lax.dynamic_slice(padded, (zero, e.astype(jnp.int32), rows, cols), (2, 1, ROWS, W))
            return total + piece[:, 0]
        sums = lax.fori_loop(0, EPOCHS, add, jnp.zeros((2, ROWS, W), jnp.float32))
        return sums[0] / jnp.sqrt(sums[1])

    def fold(best, offsets):
        return (jnp.maximum(best, one_velocity(offsets)), None)
    start = jnp.full((ROWS, W), -jnp.inf, jnp.float32)
    best, unused = lax.scan(fold, start, shifts)
    return best
```

```python
import jax
import jax.numpy as jnp
from jax import lax
from jax.experimental import pallas as pl
from jax.experimental.pallas import tpu as pltpu
from jax.sharding import PartitionSpec as P

HALO = 16
LANES = 128
CHUNK = 8


def stack_kernel(sh_ref, x_ref, lo_ref, hi_ref, out_ref, pad_ref):
    epochs, rows, slots, lanes = x_ref.shape
    blocks = slots // 2
    vels = out_ref.shape[0]

    pad_ref[:, :HALO] = lo_ref[...]
    pad_ref[:, HALO : HALO + rows] = x_ref[...]
    pad_ref[:, HALO + rows :] = hi_ref[...]

    lane = lax.broadcasted_iota(jnp.int32, (slots, lanes), 1)
    block = lax.broadcasted_iota(jnp.int32, (slots, lanes), 0) % blocks
    for v in range(vels):

        def per_chunk(rc, carry, v=v):
            row0 = rc * CHUNK

            def body(e, acc):
                at = (v * epochs + e) * 2
                s_r = sh_ref[at]
                s_c = sh_ref[at + 1]
                win = pad_ref[e, pl.ds(row0 + HALO + s_r, CHUNK)]
                rolled = pltpu.roll(win, lax.rem(lanes - s_c, lanes), axis=2)
                later = pltpu.roll(rolled, slots - 1, axis=1)
                earlier = pltpu.roll(rolled, 1, axis=1)
                moved = lane + s_c
                inside = (moved >= 0) & (moved < lanes)
                forward = (jnp.zeros((slots, lanes), jnp.int32) + s_c) >= 0
                edge = jnp.where(s_c >= 0, blocks - 1, 0)
                edge_ok = (block != edge) & ~inside
                other = jnp.where(forward[None], later, earlier)
                picked = jnp.where(inside[None], rolled, jnp.where(edge_ok[None], other, 0.0))
                return acc + picked

            init = jnp.zeros((CHUNK, slots, lanes), jnp.float32)
            acc = lax.fori_loop(0, epochs, body, init, unroll=True)
            out_ref[v, pl.ds(row0, CHUNK)] = acc
            return carry

        lax.fori_loop(0, rows // CHUNK, per_chunk, 0)


def partial_stacks(own_shifts, x, lo, hi):
    epochs, rows, slots, lanes = x.shape
    vels = own_shifts.shape[0]
    vmem = pl.BlockSpec(memory_space=pltpu.VMEM)
    return pl.pallas_call(
        stack_kernel,
        out_shape=jax.ShapeDtypeStruct((vels, rows, slots, lanes), jnp.float32),
        in_specs=[pl.BlockSpec(memory_space=pltpu.SMEM)] + [vmem] * 3,
        out_specs=vmem,
        scratch_shapes=[pltpu.VMEM((epochs, rows + 2 * HALO, slots, lanes), jnp.float32)],
        cost_estimate=pl.CostEstimate(
            flops=2 * vels * epochs * rows * slots * lanes,
            bytes_accessed=4 * (epochs * (rows + 2 * HALO) + vels * rows) * slots * lanes,
            transcendentals=0,
        ),
    )(own_shifts.reshape(-1), x, lo, hi)


def per_device(psi, phi, shifts):
    epochs, rows, cols = psi.shape
    blocks = cols // LANES
    stacked = jnp.stack([psi, phi]).reshape(2, epochs, rows, blocks, LANES)
    x = stacked.transpose(1, 2, 0, 3, 4).reshape(epochs, rows, 2 * blocks, LANES)
    count = lax.axis_size("tile")
    forward = [(i, i + 1) for i in range(count - 1)]
    backward = [(i + 1, i) for i in range(count - 1)]
    lo = lax.ppermute(x[:, rows - HALO :], "tile", forward)
    hi = lax.ppermute(x[:, :HALO], "tile", backward)
    first = lax.axis_index("epoch") * epochs
    own_shifts = lax.dynamic_slice_in_dim(shifts, first, epochs, 1)
    part = partial_stacks(own_shifts, x, lo, hi)
    vels = part.shape[0]
    part = part.reshape(vels, rows, 2, blocks, LANES).transpose(3, 0, 2, 1, 4)
    summed = lax.psum_scatter(part, "epoch", scatter_dimension=0, tiled=True)
    groups = summed.shape[0]
    summed = jnp.moveaxis(summed, 0, 3).reshape(vels, 2, rows, groups * LANES)
    ratio = summed[:, 0] / jnp.sqrt(summed[:, 1])
    return jnp.max(ratio, axis=0)


def solution(mesh):
    placed = (P("epoch", "tile", None), P("epoch", "tile", None), P())
    return jax.shard_map(
        per_device, mesh=mesh, in_specs=placed, out_specs=P("tile", "epoch"), check_vma=False
    )
```

```python
import jax
import jax.numpy as jnp
from jax import lax
from jax.experimental import pallas as pl
from jax.experimental.pallas import tpu as pltpu
from jax.sharding import PartitionSpec as P

HALO = 16
LANES = 128
CHUNK = 8


def stack_kernel(sh_ref, x_ref, lo_ref, hi_ref, out_ref, pad_ref):
    epochs, rows, slots, lanes = x_ref.shape
    blocks = slots // 2
    vels = out_ref.shape[0]

    pad_ref[:, :HALO] = lo_ref[...]
    pad_ref[:, HALO : HALO + rows] = x_ref[...]
    pad_ref[:, HALO + rows :] = hi_ref[...]

    lane = lax.broadcasted_iota(jnp.int32, (slots, lanes), 1)
    block = lax.broadcasted_iota(jnp.int32, (slots, lanes), 0) % blocks
    for v in range(vels):

        def per_chunk(rc, carry, v=v):
            row0 = rc * CHUNK

            def body(e, acc):
                at = (v * epochs + e) * 2
                s_r = sh_ref[at]
                s_c = sh_ref[at + 1]
                win = pad_ref[e, pl.ds(row0 + HALO + s_r, CHUNK)]
                rolled = pltpu.roll(win, lax.rem(lanes - s_c, lanes), axis=2)
                later = pltpu.roll(rolled, slots - 1, axis=1)
                earlier = pltpu.roll(rolled, 1, axis=1)
                moved = lane + s_c
                inside = (moved >= 0) & (moved < lanes)
                forward = (jnp.zeros((slots, lanes), jnp.int32) + s_c) >= 0
                edge = jnp.where(s_c >= 0, blocks - 1, 0)
                edge_ok = (block != edge) & ~inside
                other = jnp.where(forward[None], later, earlier)
                picked = jnp.where(inside[None], rolled, jnp.where(edge_ok[None], other, 0.0))
                return acc + picked

            init = jnp.zeros((CHUNK, slots, lanes), jnp.float32)
            acc = lax.fori_loop(0, epochs, body, init, unroll=True)
            out_ref[v, pl.ds(row0, CHUNK)] = acc
            return carry

        lax.fori_loop(0, rows // CHUNK, per_chunk, 0)


def partial_stacks(own_shifts, x, lo, hi):
    epochs, rows, slots, lanes = x.shape
    vels = own_shifts.shape[0]
    vmem = pl.BlockSpec(memory_space=pltpu.VMEM)
    return pl.pallas_call(
        stack_kernel,
        out_shape=jax.ShapeDtypeStruct((vels, rows, slots, lanes), jnp.float32),
        in_specs=[pl.BlockSpec(memory_space=pltpu.SMEM)] + [vmem] * 3,
        out_specs=vmem,
        scratch_shapes=[pltpu.VMEM((epochs, rows + 2 * HALO, slots, lanes), jnp.float32)],
        cost_estimate=pl.CostEstimate(
            flops=2 * vels * epochs * rows * slots * lanes,
            bytes_accessed=4 * (epochs * (rows + 2 * HALO) + vels * rows) * slots * lanes,
            transcendentals=0,
        ),
    )(own_shifts.reshape(-1), x, lo, hi)


def per_device(psi, phi, shifts):
    epochs, rows, cols = psi.shape
    blocks = cols // LANES
    stacked = jnp.stack([psi, phi]).reshape(2, epochs, rows, blocks, LANES)
    x = stacked.transpose(1, 2, 0, 3, 4).reshape(epochs, rows, 2 * blocks, LANES)
    count = lax.axis_size("tile")
    forward = [(i, i + 1) for i in range(count - 1)]
    backward = [(i + 1, i) for i in range(count - 1)]
    lo = lax.ppermute(x[:, rows - HALO :], "tile", forward)
    hi = lax.ppermute(x[:, :HALO], "tile", backward)
    first = lax.axis_index("epoch") * epochs
    own_shifts = lax.dynamic_slice_in_dim(shifts, first, epochs, 1)
    part = partial_stacks(own_shifts, x, lo, hi)
    vels = part.shape[0]
    part = part.reshape(vels, rows, 2, blocks, LANES).transpose(3, 0, 2, 1, 4)
    summed = ring_reduce_scatter(part, "epoch")
    ratio = summed[:, 0] / jnp.sqrt(summed[:, 1])
    return jnp.max(ratio, axis=0)


def ring_reduce_scatter(part, axis):
    n = lax.axis_size(axis)
    g = lax.axis_index(axis)
    half = part.shape[3] // 2
    ahead = [(i, (i + 1) % n) for i in range(n)]
    behind = [(i, (i - 1) % n) for i in range(n)]
    upper = part[:, :, :, :half]
    lower = part[:, :, :, half:]

    def pick(x, b):
        return lax.dynamic_index_in_dim(x, lax.rem(b + 2 * n, n), 0, keepdims=False)

    up = pick(upper, g - 1)
    down = pick(lower, g + 1)
    for s in range(1, n):
        up = lax.ppermute(up, axis, ahead) + pick(upper, g - 1 - s)
        down = lax.ppermute(down, axis, behind) + pick(lower, g + 1 + s)
    return jnp.concatenate([up, down], axis=2)


def solution(mesh):
    placed = (P("epoch", "tile", None), P("epoch", "tile", None), P())
    return jax.shard_map(
        per_device, mesh=mesh, in_specs=placed, out_specs=P("tile", "epoch"), check_vma=False
    )
```

```python
import jax
import jax.numpy as jnp
from jax import lax
from jax.experimental import pallas as pl
from jax.experimental.pallas import tpu as pltpu
from jax.sharding import PartitionSpec as P

HALO = 16
LANES = 128
CHUNK = 8


def stack_kernel(sh_ref, x_ref, lo_ref, hi_ref, out_ref, pad_ref):
    epochs, rows, slots, lanes = x_ref.shape
    blocks = slots // 2
    vels = out_ref.shape[0]

    pad_ref[:, :HALO] = lo_ref[...]
    pad_ref[:, HALO : HALO + rows] = x_ref[...]
    pad_ref[:, HALO + rows :] = hi_ref[...]

    lane = lax.broadcasted_iota(jnp.int32, (slots, lanes), 1)
    block = lax.broadcasted_iota(jnp.int32, (slots, lanes), 0) % blocks
    for v in range(vels):

        def per_chunk(rc, carry, v=v):
            row0 = rc * CHUNK

            def body(e, acc):
                at = (v * epochs + e) * 2
                s_r = sh_ref[at]
                s_c = sh_ref[at + 1]
                win = pad_ref[e, pl.ds(row0 + HALO + s_r, CHUNK)]
                rolled = pltpu.roll(win, lax.rem(lanes - s_c, lanes), axis=2)
                later = pltpu.roll(rolled, slots - 1, axis=1)
                earlier = pltpu.roll(rolled, 1, axis=1)
                moved = lane + s_c
                inside = (moved >= 0) & (moved < lanes)
                forward = (jnp.zeros((slots, lanes), jnp.int32) + s_c) >= 0
                edge = jnp.where(s_c >= 0, blocks - 1, 0)
                edge_ok = (block != edge) & ~inside
                other = jnp.where(forward[None], later, earlier)
                picked = jnp.where(inside[None], rolled, jnp.where(edge_ok[None], other, 0.0))
                return acc + picked

            init = jnp.zeros((CHUNK, slots, lanes), jnp.float32)
            acc = lax.fori_loop(0, epochs, body, init, unroll=True)
            out_ref[v, pl.ds(row0, CHUNK)] = acc
            return carry

        lax.fori_loop(0, rows // CHUNK, per_chunk, 0)


def partial_stacks(own_shifts, x, lo, hi):
    epochs, rows, slots, lanes = x.shape
    vels = own_shifts.shape[0]
    vmem = pl.BlockSpec(memory_space=pltpu.VMEM)
    return pl.pallas_call(
        stack_kernel,
        out_shape=jax.ShapeDtypeStruct((vels, rows, slots, lanes), jnp.float32),
        in_specs=[pl.BlockSpec(memory_space=pltpu.SMEM)] + [vmem] * 3,
        out_specs=vmem,
        scratch_shapes=[pltpu.VMEM((epochs, rows + 2 * HALO, slots, lanes), jnp.float32)],
        cost_estimate=pl.CostEstimate(
            flops=2 * vels * epochs * rows * slots * lanes,
            bytes_accessed=4 * (epochs * (rows + 2 * HALO) + vels * rows) * slots * lanes,
            transcendentals=0,
        ),
    )(own_shifts.reshape(-1), x, lo, hi)


def per_device(psi, phi, shifts):
    epochs, rows, cols = psi.shape
    blocks = cols // LANES
    stacked = jnp.stack([psi, phi]).reshape(2, epochs, rows, blocks, LANES)
    x = stacked.transpose(1, 2, 0, 3, 4).reshape(epochs, rows, 2 * blocks, LANES)
    count = lax.axis_size("tile")
    forward = [(i, i + 1) for i in range(count - 1)]
    backward = [(i + 1, i) for i in range(count - 1)]
    lo = lax.ppermute(x[:, rows - HALO :], "tile", forward)
    hi = lax.ppermute(x[:, :HALO], "tile", backward)
    first = lax.axis_index("epoch") * epochs
    own_shifts = lax.dynamic_slice_in_dim(shifts, first, epochs, 1)
    part = partial_stacks(own_shifts, x, lo, hi)
    vels = part.shape[0]
    part = part.reshape(vels, rows, 2, blocks, LANES).transpose(3, 0, 2, 1, 4)
    summed = jnp.sum(lax.all_to_all(part, "epoch", 0, 0, tiled=True), axis=0)
    ratio = summed[:, 0] / jnp.sqrt(summed[:, 1])
    return jnp.max(ratio, axis=0)


def ring_reduce_scatter(part, axis):
    n = lax.axis_size(axis)
    g = lax.axis_index(axis)
    half = part.shape[3] // 2
    ahead = [(i, (i + 1) % n) for i in range(n)]
    behind = [(i, (i - 1) % n) for i in range(n)]
    upper = part[:, :, :, :half]
    lower = part[:, :, :, half:]

    def pick(x, b):
        return lax.dynamic_index_in_dim(x, lax.rem(b + 2 * n, n), 0, keepdims=False)

    up = pick(upper, g - 1)
    down = pick(lower, g + 1)
    for s in range(1, n):
        up = lax.ppermute(up, axis, ahead) + pick(upper, g - 1 - s)
        down = lax.ppermute(down, axis, behind) + pick(lower, g + 1 + s)
    return jnp.concatenate([up, down], axis=2)


def solution(mesh):
    placed = (P("epoch", "tile", None), P("epoch", "tile", None), P())
    return jax.shard_map(
        per_device, mesh=mesh, in_specs=placed, out_specs=P("tile", "epoch"), check_vma=False
    )
```

```python
import jax
import jax.numpy as jnp
from jax import lax
from jax.experimental import pallas as pl
from jax.experimental.pallas import tpu as pltpu
from jax.sharding import PartitionSpec as P

HALO = 16
LANES = 128
CHUNK = 8


def stack_kernel(sh_ref, x_ref, out_ref):
    epochs, rows, slots, lanes = x_ref.shape
    blocks = slots // 2
    vels = out_ref.shape[0]

    out_ref[...] = jnp.zeros(out_ref.shape, jnp.float32)
    lane = lax.broadcasted_iota(jnp.int32, (slots, lanes), 1)
    block = lax.broadcasted_iota(jnp.int32, (slots, lanes), 0) % blocks
    for v in range(vels):

        def body(e, carry, v=v):
            at = (v * epochs + e) * 2
            s_r = sh_ref[at]
            s_c = sh_ref[at + 1]
            amount = lax.rem(lanes - s_c, lanes)
            moved = lane + s_c
            inside = (moved >= 0) & (moved < lanes)
            forward = (jnp.zeros((slots, lanes), jnp.int32) + s_c) >= 0
            edge = jnp.where(s_c >= 0, blocks - 1, 0)
            edge_ok = (block != edge) & ~inside
            for rc in range(rows // CHUNK):
                win = x_ref[e, rc * CHUNK : (rc + 1) * CHUNK]
                rolled = pltpu.roll(win, amount, axis=2)
                later = pltpu.roll(rolled, slots - 1, axis=1)
                earlier = pltpu.roll(rolled, 1, axis=1)
                other = jnp.where(forward[None], later, earlier)
                picked = jnp.where(inside[None], rolled, jnp.where(edge_ok[None], other, 0.0))
                dest = out_ref.at[v, pl.ds(HALO - s_r + rc * CHUNK, CHUNK)]
                dest[...] = dest[...] + picked
            return carry

        lax.fori_loop(0, epochs, body, 0)


def partial_stacks(own_shifts, x):
    epochs, rows, slots, lanes = x.shape
    vels = own_shifts.shape[0]
    vmem = pl.BlockSpec(memory_space=pltpu.VMEM)
    return pl.pallas_call(
        stack_kernel,
        out_shape=jax.ShapeDtypeStruct((vels, rows + 2 * HALO, slots, lanes), jnp.float32),
        in_specs=[pl.BlockSpec(memory_space=pltpu.SMEM), vmem],
        out_specs=vmem,
        cost_estimate=pl.CostEstimate(
            flops=2 * vels * epochs * rows * slots * lanes,
            bytes_accessed=4 * (epochs * rows + vels * (rows + 2 * HALO)) * slots * lanes,
            transcendentals=0,
        ),
    )(own_shifts.reshape(-1), x)


def per_device(psi, phi, shifts):
    epochs, rows, cols = psi.shape
    blocks = cols // LANES
    stacked = jnp.stack([psi, phi]).reshape(2, epochs, rows, blocks, LANES)
    x = stacked.transpose(1, 2, 0, 3, 4).reshape(epochs, rows, 2 * blocks, LANES)
    first = lax.axis_index("epoch") * epochs
    own_shifts = lax.dynamic_slice_in_dim(shifts, first, epochs, 1)
    part = partial_stacks(own_shifts, x)
    count = lax.axis_size("tile")
    forward = [(i, i + 1) for i in range(count - 1)]
    backward = [(i + 1, i) for i in range(count - 1)]
    from_above = lax.ppermute(part[:, rows + HALO :], "tile", forward)
    from_below = lax.ppermute(part[:, :HALO], "tile", backward)
    vels = part.shape[0]
    middle = jnp.zeros((vels, rows - 2 * HALO) + part.shape[2:], jnp.float32)
    part = part[:, HALO : HALO + rows] + jnp.concatenate([from_above, middle, from_below], axis=1)
    part = part.reshape(vels, rows, 2, blocks, LANES).transpose(3, 0, 2, 1, 4)
    summed = jnp.sum(lax.all_to_all(part, "epoch", 0, 0, tiled=True), axis=0)
    ratio = summed[:, 0] / jnp.sqrt(summed[:, 1])
    return jnp.max(ratio, axis=0)


def solution(mesh):
    placed = (P("epoch", "tile", None), P("epoch", "tile", None), P())
    return jax.shard_map(
        per_device, mesh=mesh, in_specs=placed, out_specs=P("tile", "epoch"), check_vma=False
    )
```

```python
import jax
import jax.numpy as jnp
from jax import lax
from jax.experimental import pallas as pl
from jax.experimental.pallas import tpu as pltpu
from jax.sharding import PartitionSpec as P

HALO = 16
LANES = 128
CHUNK = 8


def stack_kernel(sh_ref, x_ref, out_ref):
    epochs, rows, slots, lanes = x_ref.shape
    blocks = slots // 2
    vels = out_ref.shape[0]

    out_ref[...] = jnp.zeros(out_ref.shape, jnp.float32)
    lane = lax.broadcasted_iota(jnp.int32, (slots, lanes), 1)
    block = lax.broadcasted_iota(jnp.int32, (slots, lanes), 0) % blocks
    for v in range(vels):

        def body(e, carry, v=v):
            at = (v * epochs + e) * 2
            s_r = sh_ref[at]
            s_c = sh_ref[at + 1]
            amount = lax.rem(lanes - s_c, lanes)
            moved = lane + s_c
            inside = (moved >= 0) & (moved < lanes)
            step = jnp.where(s_c >= 0, slots - 1, 1)
            edge = jnp.where(s_c >= 0, blocks - 1, 0)
            edge_ok = (block != edge) & ~inside
            for rc in range(rows // CHUNK):
                win = x_ref[e, rc * CHUNK : (rc + 1) * CHUNK]
                rolled = pltpu.roll(win, amount, axis=2)
                other = pltpu.roll(rolled, step, axis=1)
                picked = jnp.where(inside[None], rolled, jnp.where(edge_ok[None], other, 0.0))
                dest = out_ref.at[v, pl.ds(HALO - s_r + rc * CHUNK, CHUNK)]
                dest[...] = dest[...] + picked
            return carry

        lax.fori_loop(0, epochs, body, 0)


def partial_stacks(own_shifts, x):
    epochs, rows, slots, lanes = x.shape
    vels = own_shifts.shape[0]
    vmem = pl.BlockSpec(memory_space=pltpu.VMEM)
    return pl.pallas_call(
        stack_kernel,
        out_shape=jax.ShapeDtypeStruct((vels, rows + 2 * HALO, slots, lanes), jnp.float32),
        in_specs=[pl.BlockSpec(memory_space=pltpu.SMEM), vmem],
        out_specs=vmem,
        cost_estimate=pl.CostEstimate(
            flops=2 * vels * epochs * rows * slots * lanes,
            bytes_accessed=4 * (epochs * rows + vels * (rows + 2 * HALO)) * slots * lanes,
            transcendentals=0,
        ),
    )(own_shifts.reshape(-1), x)


def per_device(psi, phi, shifts):
    epochs, rows, cols = psi.shape
    blocks = cols // LANES
    stacked = jnp.stack([psi, phi]).reshape(2, epochs, rows, blocks, LANES)
    x = stacked.transpose(1, 2, 0, 3, 4).reshape(epochs, rows, 2 * blocks, LANES)
    first = lax.axis_index("epoch") * epochs
    own_shifts = lax.dynamic_slice_in_dim(shifts, first, epochs, 1)
    part = partial_stacks(own_shifts, x)
    count = lax.axis_size("tile")
    forward = [(i, i + 1) for i in range(count - 1)]
    backward = [(i + 1, i) for i in range(count - 1)]
    from_above = lax.ppermute(part[:, rows + HALO :], "tile", forward)
    from_below = lax.ppermute(part[:, :HALO], "tile", backward)
    vels = part.shape[0]
    middle = jnp.zeros((vels, rows - 2 * HALO) + part.shape[2:], jnp.float32)
    part = part[:, HALO : HALO + rows] + jnp.concatenate([from_above, middle, from_below], axis=1)
    part = part.reshape(vels, rows, 2, blocks, LANES).transpose(3, 0, 2, 1, 4)
    summed = jnp.sum(lax.all_to_all(part, "epoch", 0, 0, tiled=True), axis=0)
    ratio = summed[:, 0] / jnp.sqrt(summed[:, 1])
    return jnp.max(ratio, axis=0)


def solution(mesh):
    placed = (P("epoch", "tile", None), P("epoch", "tile", None), P())
    return jax.shard_map(
        per_device, mesh=mesh, in_specs=placed, out_specs=P("tile", "epoch"), check_vma=False
    )
```

```python
import jax
import jax.numpy as jnp
from jax import lax
from jax.experimental import pallas as pl
from jax.experimental.pallas import tpu as pltpu
from jax.sharding import PartitionSpec as P

HALO = 16
LANES = 128
CHUNK = 8


def stack_kernel(sh_ref, x_ref, out_ref, odd_ref):
    epochs, rows, slots, lanes = x_ref.shape
    blocks = slots // 2
    vels = out_ref.shape[0]

    out_ref[...] = jnp.zeros(out_ref.shape, jnp.float32)
    odd_ref[...] = jnp.zeros(odd_ref.shape, jnp.float32)
    lane = lax.broadcasted_iota(jnp.int32, (slots, lanes), 1)
    block = lax.broadcasted_iota(jnp.int32, (slots, lanes), 0) % blocks
    for v in range(vels):

        def body(i, carry, v=v):
            for parity, acc_ref in ((0, out_ref), (1, odd_ref)):
                add_epoch(v, 2 * i + parity, acc_ref)
            return carry

        def add_epoch(v, e, acc_ref):
            at = (v * epochs + e) * 2
            s_r = sh_ref[at]
            s_c = sh_ref[at + 1]
            amount = lax.rem(lanes - s_c, lanes)
            moved = lane + s_c
            inside = (moved >= 0) & (moved < lanes)
            step = jnp.where(s_c >= 0, slots - 1, 1)
            edge = jnp.where(s_c >= 0, blocks - 1, 0)
            edge_ok = (block != edge) & ~inside
            for rc in range(rows // CHUNK):
                win = x_ref[e, rc * CHUNK : (rc + 1) * CHUNK]
                rolled = pltpu.roll(win, amount, axis=2)
                other = pltpu.roll(rolled, step, axis=1)
                picked = jnp.where(inside[None], rolled, jnp.where(edge_ok[None], other, 0.0))
                dest = acc_ref.at[v, pl.ds(HALO - s_r + rc * CHUNK, CHUNK)]
                dest[...] = dest[...] + picked

        lax.fori_loop(0, epochs // 2, body, 0)
        out_ref[v] = out_ref[v] + odd_ref[v]


def partial_stacks(own_shifts, x):
    epochs, rows, slots, lanes = x.shape
    vels = own_shifts.shape[0]
    vmem = pl.BlockSpec(memory_space=pltpu.VMEM)
    return pl.pallas_call(
        stack_kernel,
        out_shape=jax.ShapeDtypeStruct((vels, rows + 2 * HALO, slots, lanes), jnp.float32),
        in_specs=[pl.BlockSpec(memory_space=pltpu.SMEM), vmem],
        out_specs=vmem,
        scratch_shapes=[pltpu.VMEM((vels, rows + 2 * HALO, slots, lanes), jnp.float32)],
        cost_estimate=pl.CostEstimate(
            flops=2 * vels * epochs * rows * slots * lanes,
            bytes_accessed=4 * (epochs * rows + vels * (rows + 2 * HALO)) * slots * lanes,
            transcendentals=0,
        ),
    )(own_shifts.reshape(-1), x)


def per_device(psi, phi, shifts):
    epochs, rows, cols = psi.shape
    blocks = cols // LANES
    stacked = jnp.stack([psi, phi]).reshape(2, epochs, rows, blocks, LANES)
    x = stacked.transpose(1, 2, 0, 3, 4).reshape(epochs, rows, 2 * blocks, LANES)
    first = lax.axis_index("epoch") * epochs
    own_shifts = lax.dynamic_slice_in_dim(shifts, first, epochs, 1)
    part = partial_stacks(own_shifts, x)
    count = lax.axis_size("tile")
    forward = [(i, i + 1) for i in range(count - 1)]
    backward = [(i + 1, i) for i in range(count - 1)]
    from_above = lax.ppermute(part[:, rows + HALO :], "tile", forward)
    from_below = lax.ppermute(part[:, :HALO], "tile", backward)
    vels = part.shape[0]
    middle = jnp.zeros((vels, rows - 2 * HALO) + part.shape[2:], jnp.float32)
    part = part[:, HALO : HALO + rows] + jnp.concatenate([from_above, middle, from_below], axis=1)
    part = part.reshape(vels, rows, 2, blocks, LANES).transpose(3, 0, 2, 1, 4)
    summed = jnp.sum(lax.all_to_all(part, "epoch", 0, 0, tiled=True), axis=0)
    ratio = summed[:, 0] / jnp.sqrt(summed[:, 1])
    return jnp.max(ratio, axis=0)


def solution(mesh):
    placed = (P("epoch", "tile", None), P("epoch", "tile", None), P())
    return jax.shard_map(
        per_device, mesh=mesh, in_specs=placed, out_specs=P("tile", "epoch"), check_vma=False
    )
```

```python
import jax
import jax.numpy as jnp
from jax import lax
from jax.experimental import pallas as pl
from jax.experimental.pallas import tpu as pltpu
from jax.sharding import PartitionSpec as P

HALO = 16
LANES = 128
CHUNK = 8


def stack_kernel(sh_ref, x_ref, own_ref, top_ref, bottom_ref, acc_ref):
    epochs, rows, slots, lanes = x_ref.shape
    blocks = slots // 2
    chains = acc_ref.shape[0]
    vels = acc_ref.shape[1]
    total = sh_ref.shape[0] // (2 * vels)
    first = lax.axis_index("epoch") * epochs

    acc_ref[...] = jnp.zeros(acc_ref.shape, jnp.float32)
    lane = lax.broadcasted_iota(jnp.int32, (slots, lanes), 1)
    block = lax.broadcasted_iota(jnp.int32, (slots, lanes), 0) % blocks
    for v in range(vels):

        def add_epoch(v, e, into):
            at = (v * total + first + e) * 2
            s_r = sh_ref[at]
            s_c = sh_ref[at + 1]
            amount = lax.rem(lanes - s_c, lanes)
            moved = lane + s_c
            inside = (moved >= 0) & (moved < lanes)
            step = jnp.where(s_c >= 0, slots - 1, 1)
            edge = jnp.where(s_c >= 0, blocks - 1, 0)
            edge_ok = (block != edge) & ~inside
            for rc in range(rows // CHUNK):
                win = x_ref[e, rc * CHUNK : (rc + 1) * CHUNK]
                rolled = pltpu.roll(win, amount, axis=2)
                other = pltpu.roll(rolled, step, axis=1)
                picked = jnp.where(inside[None], rolled, jnp.where(edge_ok[None], other, 0.0))
                dest = acc_ref.at[into, v, pl.ds(HALO - s_r + rc * CHUNK, CHUNK)]
                dest[...] = dest[...] + picked

        def body(i, carry, v=v):
            for chain in range(chains):
                add_epoch(v, chains * i + chain, chain)
            return carry

        lax.fori_loop(0, epochs // chains, body, 0)
        total_v = acc_ref[0, v]
        for chain in range(1, chains):
            total_v = total_v + acc_ref[chain, v]
        top_ref[v] = total_v[:HALO]
        own_ref[v] = total_v[HALO : HALO + rows]
        bottom_ref[v] = total_v[HALO + rows :]


def partial_stacks(shifts, x):
    epochs, rows, slots, lanes = x.shape
    vels = shifts.shape[0]
    chains = 4 if epochs % 4 == 0 else (2 if epochs % 2 == 0 else 1)
    vmem = pl.BlockSpec(memory_space=pltpu.VMEM)
    spill = jax.ShapeDtypeStruct((vels, HALO, slots, lanes), jnp.float32)
    return pl.pallas_call(
        stack_kernel,
        out_shape=(jax.ShapeDtypeStruct((vels, rows, slots, lanes), jnp.float32), spill, spill),
        in_specs=[pl.BlockSpec(memory_space=pltpu.SMEM), vmem],
        out_specs=(vmem, vmem, vmem),
        scratch_shapes=[pltpu.VMEM((chains, vels, rows + 2 * HALO, slots, lanes), jnp.float32)],
        cost_estimate=pl.CostEstimate(
            flops=2 * vels * epochs * rows * slots * lanes,
            bytes_accessed=4 * (epochs * rows + vels * (rows + 2 * HALO)) * slots * lanes,
            transcendentals=0,
        ),
    )(shifts.reshape(-1), x)


def per_device(psi, phi, shifts):
    epochs, rows, cols = psi.shape
    blocks = cols // LANES
    stacked = jnp.stack([psi, phi]).reshape(2, epochs, rows, blocks, LANES)
    x = stacked.transpose(1, 2, 0, 3, 4).reshape(epochs, rows, 2 * blocks, LANES)
    own, top, bottom = partial_stacks(shifts, x)
    count = lax.axis_size("tile")
    forward = [(i, i + 1) for i in range(count - 1)]
    backward = [(i + 1, i) for i in range(count - 1)]
    from_above = lax.ppermute(bottom, "tile", forward)
    from_below = lax.ppermute(top, "tile", backward)
    vels = own.shape[0]
    middle = jnp.zeros((vels, rows - 2 * HALO) + own.shape[2:], jnp.float32)
    part = own + jnp.concatenate([from_above, middle, from_below], axis=1)
    part = part.reshape(vels, rows, 2, blocks, LANES).transpose(3, 0, 2, 1, 4)
    summed = jnp.sum(lax.all_to_all(part, "epoch", 0, 0, tiled=True), axis=0)
    ratio = summed[:, 0] / jnp.sqrt(summed[:, 1])
    return jnp.max(ratio, axis=0)


def solution(mesh):
    placed = (P("epoch", "tile", None), P("epoch", "tile", None), P())
    return jax.shard_map(
        per_device, mesh=mesh, in_specs=placed, out_specs=P("tile", "epoch"), check_vma=False
    )
```

```python
import jax
import jax.numpy as jnp
from jax import lax
from jax.experimental import pallas as pl
from jax.experimental.pallas import tpu as pltpu
from jax.sharding import PartitionSpec as P

HALO = 16
LANES = 128
CHUNK = 8


def stack_kernel(sh_ref, x_ref, own_ref, top_ref, bottom_ref, acc_ref):
    epochs, rows, slots, lanes = x_ref.shape
    blocks = slots // 2
    vels = acc_ref.shape[0]
    first = lax.axis_index("epoch") * epochs

    acc_ref[...] = jnp.zeros(acc_ref.shape, jnp.float32)
    lane = lax.broadcasted_iota(jnp.int32, (slots, lanes), 1)
    block = lax.broadcasted_iota(jnp.int32, (slots, lanes), 0) % blocks

    def add_epoch(v, e):
        s_r = sh_ref[v, first + e, 0]
        s_c = sh_ref[v, first + e, 1]
        amount = lax.rem(lanes - s_c, lanes)
        moved = lane + s_c
        inside = (moved >= 0) & (moved < lanes)
        step = jnp.where(s_c >= 0, slots - 1, 1)
        edge = jnp.where(s_c >= 0, blocks - 1, 0)
        edge_ok = (block != edge) & ~inside
        for rc in range(rows // CHUNK):
            win = x_ref[e, rc * CHUNK : (rc + 1) * CHUNK]
            rolled = pltpu.roll(win, amount, axis=2)
            other = pltpu.roll(rolled, step, axis=1)
            picked = jnp.where(inside[None], rolled, jnp.where(edge_ok[None], other, 0.0))
            dest = acc_ref.at[v, pl.ds(HALO - s_r + rc * CHUNK, CHUNK)]
            dest[...] = dest[...] + picked

    def body(e, carry):
        for v in range(vels):
            add_epoch(v, e)
        return carry

    lax.fori_loop(0, epochs, body, 0)
    for v in range(vels):
        top_ref[v] = acc_ref[v, :HALO]
        own_ref[v] = acc_ref[v, HALO : HALO + rows]
        bottom_ref[v] = acc_ref[v, HALO + rows :]


def partial_stacks(shifts, x):
    epochs, rows, slots, lanes = x.shape
    vels = shifts.shape[0]
    vmem = pl.BlockSpec(memory_space=pltpu.VMEM)
    spill = jax.ShapeDtypeStruct((vels, HALO, slots, lanes), jnp.float32)
    return pl.pallas_call(
        stack_kernel,
        out_shape=(jax.ShapeDtypeStruct((vels, rows, slots, lanes), jnp.float32), spill, spill),
        in_specs=[pl.BlockSpec(memory_space=pltpu.SMEM), vmem],
        out_specs=(vmem, vmem, vmem),
        scratch_shapes=[pltpu.VMEM((vels, rows + 2 * HALO, slots, lanes), jnp.float32)],
        cost_estimate=pl.CostEstimate(
            flops=2 * vels * epochs * rows * slots * lanes,
            bytes_accessed=4 * (epochs * rows + vels * (rows + 2 * HALO)) * slots * lanes,
            transcendentals=0,
        ),
    )(shifts, x)


def per_device(psi, phi, shifts):
    epochs, rows, cols = psi.shape
    blocks = cols // LANES
    stacked = jnp.stack([psi, phi]).reshape(2, epochs, rows, blocks, LANES)
    x = stacked.transpose(1, 2, 0, 3, 4).reshape(epochs, rows, 2 * blocks, LANES)
    own, top, bottom = partial_stacks(shifts, x)
    count = lax.axis_size("tile")
    forward = [(i, i + 1) for i in range(count - 1)]
    backward = [(i + 1, i) for i in range(count - 1)]
    from_above = lax.ppermute(bottom, "tile", forward)
    from_below = lax.ppermute(top, "tile", backward)
    vels = own.shape[0]
    middle = jnp.zeros((vels, rows - 2 * HALO) + own.shape[2:], jnp.float32)
    part = own + jnp.concatenate([from_above, middle, from_below], axis=1)
    part = part.reshape(vels, rows, 2, blocks, LANES).transpose(3, 0, 2, 1, 4)
    summed = jnp.sum(lax.all_to_all(part, "epoch", 0, 0, tiled=True), axis=0)
    ratio = summed[:, 0] / jnp.sqrt(summed[:, 1])
    return jnp.max(ratio, axis=0)


def solution(mesh):
    placed = (P("epoch", "tile", None), P("epoch", "tile", None), P())
    return jax.shard_map(
        per_device, mesh=mesh, in_specs=placed, out_specs=P("tile", "epoch"), check_vma=False
    )
```

```python
import jax
import jax.numpy as jnp
from jax import lax
from jax.experimental import pallas as pl
from jax.experimental.pallas import tpu as pltpu
from jax.sharding import PartitionSpec as P

HALO = 16
LANES = 128
CHUNK = 8


def stack_kernel(sh_ref, x_ref, own_ref, top_ref, bottom_ref, acc_ref):
    epochs, rows, slots, lanes = x_ref.shape
    blocks = slots // 2
    chains = acc_ref.shape[0]
    vels = acc_ref.shape[1]
    first = lax.axis_index("epoch") * epochs

    acc_ref[...] = jnp.zeros(acc_ref.shape, jnp.float32)
    lane = lax.broadcasted_iota(jnp.int32, (slots, lanes), 1)
    block = lax.broadcasted_iota(jnp.int32, (slots, lanes), 0) % blocks
    for v in range(vels):

        def add_epoch(v, e, into):
            s_r = sh_ref[v, first + e, 0]
            s_c = sh_ref[v, first + e, 1]
            amount = lax.rem(lanes - s_c, lanes)
            moved = lane + s_c
            inside = (moved >= 0) & (moved < lanes)
            step = jnp.where(s_c >= 0, slots - 1, 1)
            edge = jnp.where(s_c >= 0, blocks - 1, 0)
            edge_ok = (block != edge) & ~inside
            for rc in range(rows // CHUNK):
                win = x_ref[e, rc * CHUNK : (rc + 1) * CHUNK]
                rolled = pltpu.roll(win, amount, axis=2)
                other = pltpu.roll(rolled, step, axis=1)
                picked = jnp.where(inside[None], rolled, jnp.where(edge_ok[None], other, 0.0))
                dest = acc_ref.at[into, v, pl.ds(HALO - s_r + rc * CHUNK, CHUNK)]
                dest[...] = dest[...] + picked

        def body(i, carry, v=v):
            for chain in range(chains):
                add_epoch(v, chains * i + chain, chain)
            return carry

        lax.fori_loop(0, epochs // chains, body, 0)
        total_v = acc_ref[0, v]
        for chain in range(1, chains):
            total_v = total_v + acc_ref[chain, v]
        top_ref[v] = total_v[:HALO]
        own_ref[v] = total_v[HALO : HALO + rows]
        bottom_ref[v] = total_v[HALO + rows :]


def partial_stacks(shifts, x):
    epochs, rows, slots, lanes = x.shape
    vels = shifts.shape[0]
    chains = 4 if epochs % 4 == 0 else (2 if epochs % 2 == 0 else 1)
    vmem = pl.BlockSpec(memory_space=pltpu.VMEM)
    spill = jax.ShapeDtypeStruct((vels, HALO, slots, lanes), jnp.float32)
    return pl.pallas_call(
        stack_kernel,
        out_shape=(jax.ShapeDtypeStruct((vels, rows, slots, lanes), jnp.float32), spill, spill),
        in_specs=[pl.BlockSpec(memory_space=pltpu.SMEM), vmem],
        out_specs=(vmem, vmem, vmem),
        scratch_shapes=[pltpu.VMEM((chains, vels, rows + 2 * HALO, slots, lanes), jnp.float32)],
        cost_estimate=pl.CostEstimate(
            flops=2 * vels * epochs * rows * slots * lanes,
            bytes_accessed=4 * (epochs * rows + vels * (rows + 2 * HALO)) * slots * lanes,
            transcendentals=0,
        ),
    )(shifts, x)


def per_device(psi, phi, shifts):
    epochs, rows, cols = psi.shape
    blocks = cols // LANES
    stacked = jnp.stack([psi, phi]).reshape(2, epochs, rows, blocks, LANES)
    x = stacked.transpose(1, 2, 0, 3, 4).reshape(epochs, rows, 2 * blocks, LANES)
    own, top, bottom = partial_stacks(shifts, x)
    count = lax.axis_size("tile")
    forward = [(i, i + 1) for i in range(count - 1)]
    backward = [(i + 1, i) for i in range(count - 1)]
    from_above = lax.ppermute(bottom, "tile", forward)
    from_below = lax.ppermute(top, "tile", backward)
    vels = own.shape[0]
    middle = jnp.zeros((vels, rows - 2 * HALO) + own.shape[2:], jnp.float32)
    part = own + jnp.concatenate([from_above, middle, from_below], axis=1)
    part = part.reshape(vels, rows, 2, blocks, LANES).transpose(3, 0, 2, 1, 4)
    summed = jnp.sum(lax.all_to_all(part, "epoch", 0, 0, tiled=True), axis=0)
    ratio = summed[:, 0] / jnp.sqrt(summed[:, 1])
    return jnp.max(ratio, axis=0)


def solution(mesh):
    placed = (P("epoch", "tile", None), P("epoch", "tile", None), P())
    return jax.shard_map(
        per_device, mesh=mesh, in_specs=placed, out_specs=P("tile", "epoch"), check_vma=False
    )
```

```python
import jax
import jax.numpy as jnp
from jax import lax
from jax.experimental import pallas as pl
from jax.experimental.pallas import tpu as pltpu
from jax.sharding import PartitionSpec as P

HALO = 16
LANES = 128
CHUNK = 8


def stack_kernel(sh_ref, x_ref, own_ref, top_ref, bottom_ref, acc_ref):
    epochs, rows, slots, lanes = x_ref.shape
    blocks = slots // 2
    vels = acc_ref.shape[0]
    total = sh_ref.shape[0] // (2 * vels)
    first = lax.axis_index("epoch") * epochs

    acc_ref[...] = jnp.zeros(acc_ref.shape, jnp.float32)
    lane = lax.broadcasted_iota(jnp.int32, (slots, lanes), 1)
    block = lax.broadcasted_iota(jnp.int32, (slots, lanes), 0) % blocks

    def add_epoch(v, e):
        at = (v * total + first + e) * 2
        s_r = sh_ref[at]
        s_c = sh_ref[at + 1]
        amount = lax.rem(lanes - s_c, lanes)
        moved = lane + s_c
        inside = (moved >= 0) & (moved < lanes)
        step = jnp.where(s_c >= 0, slots - 1, 1)
        edge = jnp.where(s_c >= 0, blocks - 1, 0)
        edge_ok = (block != edge) & ~inside
        for rc in range(rows // CHUNK):
            win = x_ref[e, rc * CHUNK : (rc + 1) * CHUNK]
            rolled = pltpu.roll(win, amount, axis=2)
            other = pltpu.roll(rolled, step, axis=1)
            picked = jnp.where(inside[None], rolled, jnp.where(edge_ok[None], other, 0.0))
            dest = acc_ref.at[v, pl.ds(HALO - s_r + rc * CHUNK, CHUNK)]
            dest[...] = dest[...] + picked

    def body(e, carry):
        for v in range(vels):
            add_epoch(v, e)
        return carry

    lax.fori_loop(0, epochs, body, 0)
    for v in range(vels):
        top_ref[v] = acc_ref[v, :HALO]
        own_ref[v] = acc_ref[v, HALO : HALO + rows]
        bottom_ref[v] = acc_ref[v, HALO + rows :]


def partial_stacks(shifts, x):
    epochs, rows, slots, lanes = x.shape
    vels = shifts.shape[0]
    vmem = pl.BlockSpec(memory_space=pltpu.VMEM)
    spill = jax.ShapeDtypeStruct((vels, HALO, slots, lanes), jnp.float32)
    return pl.pallas_call(
        stack_kernel,
        out_shape=(jax.ShapeDtypeStruct((vels, rows, slots, lanes), jnp.float32), spill, spill),
        in_specs=[pl.BlockSpec(memory_space=pltpu.SMEM), vmem],
        out_specs=(vmem, vmem, vmem),
        scratch_shapes=[pltpu.VMEM((vels, rows + 2 * HALO, slots, lanes), jnp.float32)],
        cost_estimate=pl.CostEstimate(
            flops=2 * vels * epochs * rows * slots * lanes,
            bytes_accessed=4 * (epochs * rows + vels * (rows + 2 * HALO)) * slots * lanes,
            transcendentals=0,
        ),
    )(shifts.reshape(-1), x)


def per_device(psi, phi, shifts):
    epochs, rows, cols = psi.shape
    blocks = cols // LANES
    stacked = jnp.stack([psi, phi]).reshape(2, epochs, rows, blocks, LANES)
    x = stacked.transpose(1, 2, 0, 3, 4).reshape(epochs, rows, 2 * blocks, LANES)
    own, top, bottom = partial_stacks(shifts, x)
    count = lax.axis_size("tile")
    forward = [(i, i + 1) for i in range(count - 1)]
    backward = [(i + 1, i) for i in range(count - 1)]
    from_above = lax.ppermute(bottom, "tile", forward)
    from_below = lax.ppermute(top, "tile", backward)
    vels = own.shape[0]
    middle = jnp.zeros((vels, rows - 2 * HALO) + own.shape[2:], jnp.float32)
    part = own + jnp.concatenate([from_above, middle, from_below], axis=1)
    part = part.reshape(vels, rows, 2, blocks, LANES).transpose(3, 0, 2, 1, 4)
    summed = jnp.sum(lax.all_to_all(part, "epoch", 0, 0, tiled=True), axis=0)
    ratio = summed[:, 0] / jnp.sqrt(summed[:, 1])
    return jnp.max(ratio, axis=0)


def solution(mesh):
    placed = (P("epoch", "tile", None), P("epoch", "tile", None), P())
    return jax.shard_map(
        per_device, mesh=mesh, in_specs=placed, out_specs=P("tile", "epoch"), check_vma=False
    )
```

```python
import jax
import jax.numpy as jnp
from jax import lax
from jax.experimental import pallas as pl
from jax.experimental.pallas import tpu as pltpu
from jax.sharding import PartitionSpec as P

HALO = 16
LANES = 128
CHUNK = 8


def stack_kernel(sh_ref, x_ref, own_ref, top_ref, bottom_ref, acc_ref):
    epochs, rows, slots, lanes = x_ref.shape
    blocks = slots // 2
    vels = acc_ref.shape[0]
    total = sh_ref.shape[0] // (2 * vels)
    first = lax.axis_index("epoch") * epochs

    acc_ref[...] = jnp.zeros(acc_ref.shape, jnp.float32)
    lane = lax.broadcasted_iota(jnp.int32, (slots, lanes), 1)
    block = lax.broadcasted_iota(jnp.int32, (slots, lanes), 0) % blocks

    def add_epoch(v, e):
        at = (v * total + first + e) * 2
        s_r = sh_ref[at]
        s_c = sh_ref[at + 1]
        amount = lax.rem(lanes - s_c, lanes)
        moved = lane + s_c
        inside = (moved >= 0) & (moved < lanes)
        step = jnp.where(s_c >= 0, slots - 1, 1)
        edge = jnp.where(s_c >= 0, blocks - 1, 0)
        edge_ok = (block != edge) & ~inside
        for rc in range(rows // CHUNK):
            win = x_ref[e, rc * CHUNK : (rc + 1) * CHUNK]
            rolled = pltpu.roll(win, amount, axis=2)
            other = pltpu.roll(rolled, step, axis=1)
            picked = jnp.where(inside[None], rolled, jnp.where(edge_ok[None], other, 0.0))
            dest = acc_ref.at[v, pl.ds(HALO - s_r + rc * CHUNK, CHUNK)]
            dest[...] = dest[...] + picked

    def body(e, carry):
        for v in range(vels):
            add_epoch(v, e)
        return carry

    lax.fori_loop(0, epochs, body, 0, unroll=2)
    for v in range(vels):
        top_ref[v] = acc_ref[v, :HALO]
        own_ref[v] = acc_ref[v, HALO : HALO + rows]
        bottom_ref[v] = acc_ref[v, HALO + rows :]


def partial_stacks(shifts, x):
    epochs, rows, slots, lanes = x.shape
    vels = shifts.shape[0]
    vmem = pl.BlockSpec(memory_space=pltpu.VMEM)
    spill = jax.ShapeDtypeStruct((vels, HALO, slots, lanes), jnp.float32)
    return pl.pallas_call(
        stack_kernel,
        out_shape=(jax.ShapeDtypeStruct((vels, rows, slots, lanes), jnp.float32), spill, spill),
        in_specs=[pl.BlockSpec(memory_space=pltpu.SMEM), vmem],
        out_specs=(vmem, vmem, vmem),
        scratch_shapes=[pltpu.VMEM((vels, rows + 2 * HALO, slots, lanes), jnp.float32)],
        cost_estimate=pl.CostEstimate(
            flops=2 * vels * epochs * rows * slots * lanes,
            bytes_accessed=4 * (epochs * rows + vels * (rows + 2 * HALO)) * slots * lanes,
            transcendentals=0,
        ),
    )(shifts.reshape(-1), x)


def per_device(psi, phi, shifts):
    epochs, rows, cols = psi.shape
    blocks = cols // LANES
    stacked = jnp.stack([psi, phi]).reshape(2, epochs, rows, blocks, LANES)
    x = stacked.transpose(1, 2, 0, 3, 4).reshape(epochs, rows, 2 * blocks, LANES)
    own, top, bottom = partial_stacks(shifts, x)
    count = lax.axis_size("tile")
    forward = [(i, i + 1) for i in range(count - 1)]
    backward = [(i + 1, i) for i in range(count - 1)]
    from_above = lax.ppermute(bottom, "tile", forward)
    from_below = lax.ppermute(top, "tile", backward)
    vels = own.shape[0]
    middle = jnp.zeros((vels, rows - 2 * HALO) + own.shape[2:], jnp.float32)
    part = own + jnp.concatenate([from_above, middle, from_below], axis=1)
    part = part.reshape(vels, rows, 2, blocks, LANES).transpose(3, 0, 2, 1, 4)
    gathered = lax.all_to_all(part, "epoch", 0, 0, tiled=True)
    best = None
    for v in range(vels):
        psi_sum = gathered[0, v, 0]
        phi_sum = gathered[0, v, 1]
        for source in range(1, gathered.shape[0]):
            psi_sum = psi_sum + gathered[source, v, 0]
            phi_sum = phi_sum + gathered[source, v, 1]
        ratio = psi_sum / jnp.sqrt(phi_sum)
        best = ratio if best is None else jnp.maximum(best, ratio)
    return best


def solution(mesh):
    placed = (P("epoch", "tile", None), P("epoch", "tile", None), P())
    return jax.shard_map(
        per_device, mesh=mesh, in_specs=placed, out_specs=P("tile", "epoch"), check_vma=False
    )
```

```python
import jax
import jax.numpy as jnp
from jax import lax
from jax.experimental import pallas as pl
from jax.experimental.pallas import tpu as pltpu
from jax.sharding import PartitionSpec as P

HALO = 16
LANES = 128
CHUNK = 8


def stack_kernel(sh_ref, x_ref, own_ref, top_ref, bottom_ref, acc_ref):
    epochs, rows, slots, lanes = x_ref.shape
    blocks = slots // 2
    vels = acc_ref.shape[0]
    total = sh_ref.shape[0] // (2 * vels)
    first = lax.axis_index("epoch") * epochs

    acc_ref[...] = jnp.zeros(acc_ref.shape, jnp.float32)
    lane = lax.broadcasted_iota(jnp.int32, (slots, lanes), 1)
    block = lax.broadcasted_iota(jnp.int32, (slots, lanes), 0) % blocks

    def add_epoch(v, e):
        at = v * 2 * total + first + e
        s_r = sh_ref[at]
        s_c = sh_ref[at + total]
        amount = lax.rem(lanes - s_c, lanes)
        moved = lane + s_c
        inside = (moved >= 0) & (moved < lanes)
        step = jnp.where(s_c >= 0, slots - 1, 1)
        edge = jnp.where(s_c >= 0, blocks - 1, 0)
        edge_ok = (block != edge) & ~inside
        for rc in range(rows // CHUNK):
            win = x_ref[e, rc * CHUNK : (rc + 1) * CHUNK]
            rolled = pltpu.roll(win, amount, axis=2)
            other = pltpu.roll(rolled, step, axis=1)
            picked = jnp.where(inside[None], rolled, jnp.where(edge_ok[None], other, 0.0))
            dest = acc_ref.at[v, pl.ds(HALO - s_r + rc * CHUNK, CHUNK)]
            dest[...] = dest[...] + picked

    def body(e, carry):
        for v in range(vels):
            add_epoch(v, e)
        return carry

    lax.fori_loop(0, epochs, body, 0, unroll=2)
    for v in range(vels):
        top_ref[v] = acc_ref[v, :HALO]
        own_ref[v] = acc_ref[v, HALO : HALO + rows]
        bottom_ref[v] = acc_ref[v, HALO + rows :]


def partial_stacks(shifts, x):
    epochs, rows, slots, lanes = x.shape
    vels = shifts.shape[0]
    vmem = pl.BlockSpec(memory_space=pltpu.VMEM)
    spill = jax.ShapeDtypeStruct((vels, HALO, slots, lanes), jnp.float32)
    return pl.pallas_call(
        stack_kernel,
        out_shape=(jax.ShapeDtypeStruct((vels, rows, slots, lanes), jnp.float32), spill, spill),
        in_specs=[pl.BlockSpec(memory_space=pltpu.SMEM), vmem],
        out_specs=(vmem, vmem, vmem),
        scratch_shapes=[pltpu.VMEM((vels, rows + 2 * HALO, slots, lanes), jnp.float32)],
        cost_estimate=pl.CostEstimate(
            flops=2 * vels * epochs * rows * slots * lanes,
            bytes_accessed=4 * (epochs * rows + vels * (rows + 2 * HALO)) * slots * lanes,
            transcendentals=0,
        ),
    )(jnp.swapaxes(shifts, 1, 2).reshape(-1), x)


def per_device(psi, phi, shifts):
    epochs, rows, cols = psi.shape
    blocks = cols // LANES
    stacked = jnp.stack([psi, phi]).reshape(2, epochs, rows, blocks, LANES)
    x = stacked.transpose(1, 2, 0, 3, 4).reshape(epochs, rows, 2 * blocks, LANES)
    own, top, bottom = partial_stacks(shifts, x)
    count = lax.axis_size("tile")
    forward = [(i, i + 1) for i in range(count - 1)]
    backward = [(i + 1, i) for i in range(count - 1)]
    from_above = lax.ppermute(bottom, "tile", forward)
    from_below = lax.ppermute(top, "tile", backward)
    vels = own.shape[0]
    middle = jnp.zeros((vels, rows - 2 * HALO) + own.shape[2:], jnp.float32)
    part = own + jnp.concatenate([from_above, middle, from_below], axis=1)
    part = part.reshape(vels, rows, 2, blocks, LANES).transpose(3, 0, 2, 1, 4)
    gathered = lax.all_to_all(part, "epoch", 0, 0, tiled=True)
    best = None
    for v in range(vels):
        psi_sum = gathered[0, v, 0]
        phi_sum = gathered[0, v, 1]
        for source in range(1, gathered.shape[0]):
            psi_sum = psi_sum + gathered[source, v, 0]
            phi_sum = phi_sum + gathered[source, v, 1]
        ratio = psi_sum / jnp.sqrt(phi_sum)
        best = ratio if best is None else jnp.maximum(best, ratio)
    return best


def solution(mesh):
    placed = (P("epoch", "tile", None), P("epoch", "tile", None), P())
    return jax.shard_map(
        per_device, mesh=mesh, in_specs=placed, out_specs=P("tile", "epoch"), check_vma=False
    )
```

```python
import jax
import jax.numpy as jnp
from jax import lax
from jax.experimental import pallas as pl
from jax.experimental.pallas import tpu as pltpu
from jax.sharding import PartitionSpec as P

HALO = 16
LANES = 128
CHUNK = 8


def stack_kernel(sh_ref, psi_ref, phi_ref, own_ref, top_ref, bottom_ref, acc_ref, x_ref):
    epochs, rows, slots, lanes = x_ref.shape
    blocks = slots // 2

    def pack(e, carry):
        for a in range(rows // CHUNK):
            here = slice(a * CHUNK, (a + 1) * CHUNK)
            pieces = [
                src[e, here, j * lanes : (j + 1) * lanes]
                for src in (psi_ref, phi_ref)
                for j in range(blocks)
            ]
            x_ref[e, here] = jnp.swapaxes(jnp.stack(pieces, axis=0), 0, 1)
        return carry

    lax.fori_loop(0, epochs, pack, 0)
    vels = acc_ref.shape[0]
    total = sh_ref.shape[0] // (2 * vels)
    first = lax.axis_index("epoch") * epochs

    acc_ref[...] = jnp.zeros(acc_ref.shape, jnp.float32)
    lane = lax.broadcasted_iota(jnp.int32, (slots, lanes), 1)
    block = lax.broadcasted_iota(jnp.int32, (slots, lanes), 0) % blocks

    def add_epoch(v, e):
        at = v * 2 * total + first + e
        s_r = sh_ref[at]
        s_c = sh_ref[at + total]
        amount = lax.rem(lanes - s_c, lanes)
        moved = lane + s_c
        inside = (moved >= 0) & (moved < lanes)
        step = jnp.where(s_c >= 0, slots - 1, 1)
        edge = jnp.where(s_c >= 0, blocks - 1, 0)
        edge_ok = (block != edge) & ~inside
        for rc in range(rows // CHUNK):
            win = x_ref[e, rc * CHUNK : (rc + 1) * CHUNK]
            rolled = pltpu.roll(win, amount, axis=2)
            other = pltpu.roll(rolled, step, axis=1)
            picked = jnp.where(inside[None], rolled, jnp.where(edge_ok[None], other, 0.0))
            dest = acc_ref.at[v, pl.ds(HALO - s_r + rc * CHUNK, CHUNK)]
            dest[...] = dest[...] + picked

    def body(e, carry):
        for v in range(vels):
            add_epoch(v, e)
        return carry

    lax.fori_loop(0, epochs, body, 0, unroll=2)
    for v in range(vels):
        top_ref[v] = acc_ref[v, :HALO]
        own_ref[v] = acc_ref[v, HALO : HALO + rows]
        bottom_ref[v] = acc_ref[v, HALO + rows :]


def partial_stacks(shifts, psi, phi):
    epochs, rows, cols = psi.shape
    slots, lanes = 2 * (cols // LANES), LANES
    vels = shifts.shape[0]
    vmem = pl.BlockSpec(memory_space=pltpu.VMEM)
    spill = jax.ShapeDtypeStruct((vels, HALO, slots, lanes), jnp.float32)
    return pl.pallas_call(
        stack_kernel,
        out_shape=(jax.ShapeDtypeStruct((vels, rows, slots, lanes), jnp.float32), spill, spill),
        in_specs=[pl.BlockSpec(memory_space=pltpu.SMEM), vmem, vmem],
        out_specs=(vmem, vmem, vmem),
        scratch_shapes=[
            pltpu.VMEM((vels, rows + 2 * HALO, slots, lanes), jnp.float32),
            pltpu.VMEM((epochs, rows, slots, lanes), jnp.float32),
        ],
        cost_estimate=pl.CostEstimate(
            flops=2 * vels * epochs * rows * slots * lanes,
            bytes_accessed=4 * (epochs * rows + vels * (rows + 2 * HALO)) * slots * lanes,
            transcendentals=0,
        ),
    )(jnp.swapaxes(shifts, 1, 2).reshape(-1), psi, phi)


def per_device(psi, phi, shifts):
    epochs, rows, cols = psi.shape
    blocks = cols // LANES
    own, top, bottom = partial_stacks(shifts, psi, phi)
    count = lax.axis_size("tile")
    forward = [(i, i + 1) for i in range(count - 1)]
    backward = [(i + 1, i) for i in range(count - 1)]
    from_above = lax.ppermute(bottom, "tile", forward)
    from_below = lax.ppermute(top, "tile", backward)
    vels = own.shape[0]
    middle = jnp.zeros((vels, rows - 2 * HALO) + own.shape[2:], jnp.float32)
    part = own + jnp.concatenate([from_above, middle, from_below], axis=1)
    part = part.reshape(vels, rows, 2, blocks, LANES).transpose(3, 0, 2, 1, 4)
    gathered = lax.all_to_all(part, "epoch", 0, 0, tiled=True)
    best = None
    for v in range(vels):
        psi_sum = gathered[0, v, 0]
        phi_sum = gathered[0, v, 1]
        for source in range(1, gathered.shape[0]):
            psi_sum = psi_sum + gathered[source, v, 0]
            phi_sum = phi_sum + gathered[source, v, 1]
        ratio = psi_sum / jnp.sqrt(phi_sum)
        best = ratio if best is None else jnp.maximum(best, ratio)
    return best


def solution(mesh):
    placed = (P("epoch", "tile", None), P("epoch", "tile", None), P())
    return jax.shard_map(
        per_device, mesh=mesh, in_specs=placed, out_specs=P("tile", "epoch"), check_vma=False
    )
```

```python
import jax
import jax.numpy as jnp
from jax import lax
from jax.experimental import pallas as pl
from jax.experimental.pallas import tpu as pltpu
from jax.sharding import PartitionSpec as P

HALO = 16
LANES = 128
CHUNK = 8


def stack_kernel(sh_ref, psi_ref, phi_ref, own_ref, top_ref, bottom_ref, acc_ref, x_ref):
    epochs, rows, slots, lanes = x_ref.shape
    blocks = slots // 2

    def pack(e, carry):
        for a in range(rows // CHUNK):
            here = slice(a * CHUNK, (a + 1) * CHUNK)
            pieces = [
                src[e, here, j * lanes : (j + 1) * lanes]
                for src in (psi_ref, phi_ref)
                for j in range(blocks)
            ]
            x_ref[e, here] = jnp.swapaxes(jnp.stack(pieces, axis=0), 0, 1)
        return carry

    lax.fori_loop(0, epochs, pack, 0)
    vels = acc_ref.shape[0]
    total = sh_ref.shape[0] // (2 * vels)
    first = lax.axis_index("epoch") * epochs

    acc_ref[...] = jnp.zeros(acc_ref.shape, jnp.float32)
    lane = lax.broadcasted_iota(jnp.int32, (slots, lanes), 1)
    block = lax.broadcasted_iota(jnp.int32, (slots, lanes), 0) % blocks

    def add_epoch(v, e):
        at = v * 2 * total + first + e
        s_r = sh_ref[at]
        s_c = sh_ref[at + total]
        amount = lax.rem(lanes - s_c, lanes)
        moved = lane + s_c
        inside = (moved >= 0) & (moved < lanes)
        step = jnp.where(s_c >= 0, slots - 1, 1)
        edge = jnp.where(s_c >= 0, blocks - 1, 0)
        edge_ok = (block != edge) & ~inside
        for rc in range(rows // CHUNK):
            win = x_ref[e, rc * CHUNK : (rc + 1) * CHUNK]
            rolled = pltpu.roll(win, amount, axis=2)
            other = pltpu.roll(rolled, step, axis=1)
            picked = jnp.where(inside[None], rolled, jnp.where(edge_ok[None], other, 0.0))
            dest = acc_ref.at[v, pl.ds(HALO - s_r + rc * CHUNK, CHUNK)]
            dest[...] = dest[...] + picked

    def body(e, carry):
        for v in range(vels):
            add_epoch(v, e)
        return carry

    lax.fori_loop(0, epochs, body, 0, unroll=4)
    for v in range(vels):
        top_ref[v] = acc_ref[v, :HALO]
        own_ref[v] = acc_ref[v, HALO : HALO + rows]
        bottom_ref[v] = acc_ref[v, HALO + rows :]


def partial_stacks(shifts, psi, phi):
    epochs, rows, cols = psi.shape
    slots, lanes = 2 * (cols // LANES), LANES
    vels = shifts.shape[0]
    vmem = pl.BlockSpec(memory_space=pltpu.VMEM)
    spill = jax.ShapeDtypeStruct((vels, HALO, slots, lanes), jnp.float32)
    return pl.pallas_call(
        stack_kernel,
        out_shape=(jax.ShapeDtypeStruct((vels, rows, slots, lanes), jnp.float32), spill, spill),
        in_specs=[pl.BlockSpec(memory_space=pltpu.SMEM), vmem, vmem],
        out_specs=(vmem, vmem, vmem),
        scratch_shapes=[
            pltpu.VMEM((vels, rows + 2 * HALO, slots, lanes), jnp.float32),
            pltpu.VMEM((epochs, rows, slots, lanes), jnp.float32),
        ],
        cost_estimate=pl.CostEstimate(
            flops=2 * vels * epochs * rows * slots * lanes,
            bytes_accessed=4 * (epochs * rows + vels * (rows + 2 * HALO)) * slots * lanes,
            transcendentals=0,
        ),
    )(jnp.swapaxes(shifts, 1, 2).reshape(-1), psi, phi)


def per_device(psi, phi, shifts):
    epochs, rows, cols = psi.shape
    blocks = cols // LANES
    own, top, bottom = partial_stacks(shifts, psi, phi)
    count = lax.axis_size("tile")
    forward = [(i, i + 1) for i in range(count - 1)]
    backward = [(i + 1, i) for i in range(count - 1)]
    from_above = lax.ppermute(bottom, "tile", forward)
    from_below = lax.ppermute(top, "tile", backward)
    vels = own.shape[0]
    middle = jnp.zeros((vels, rows - 2 * HALO) + own.shape[2:], jnp.float32)
    part = own + jnp.concatenate([from_above, middle, from_below], axis=1)
    part = part.reshape(vels, rows, 2, blocks, LANES).transpose(3, 0, 2, 1, 4)
    gathered = lax.all_to_all(part, "epoch", 0, 0, tiled=True)
    best = None
    for v in range(vels):
        psi_sum = gathered[0, v, 0]
        phi_sum = gathered[0, v, 1]
        for source in range(1, gathered.shape[0]):
            psi_sum = psi_sum + gathered[source, v, 0]
            phi_sum = phi_sum + gathered[source, v, 1]
        ratio = psi_sum / jnp.sqrt(phi_sum)
        best = ratio if best is None else jnp.maximum(best, ratio)
    return best


def solution(mesh):
    placed = (P("epoch", "tile", None), P("epoch", "tile", None), P())
    return jax.shard_map(
        per_device, mesh=mesh, in_specs=placed, out_specs=P("tile", "epoch"), check_vma=False
    )
```

```python
import jax
import jax.numpy as jnp
from jax import lax
from jax.experimental import pallas as pl
from jax.experimental.pallas import tpu as pltpu
from jax.sharding import PartitionSpec as P

HALO = 16
LANES = 128
CHUNK = 8


def stack_kernel(sh_ref, psi_ref, phi_ref, own_ref, top_ref, bottom_ref, acc_ref, x_ref):
    epochs, rows, slots, lanes = x_ref.shape
    blocks = slots // 2

    def pack(e, carry):
        for a in range(rows // CHUNK):
            here = slice(a * CHUNK, (a + 1) * CHUNK)
            pieces = [
                src[e, here, j * lanes : (j + 1) * lanes]
                for src in (psi_ref, phi_ref)
                for j in range(blocks)
            ]
            x_ref[e, here] = jnp.swapaxes(jnp.stack(pieces, axis=0), 0, 1)
        return carry

    lax.fori_loop(0, epochs, pack, 0)
    vels = acc_ref.shape[0]
    total = sh_ref.shape[0] // (2 * vels)
    first = lax.axis_index("epoch") * epochs

    acc_ref[...] = jnp.zeros(acc_ref.shape, jnp.float32)
    lane = lax.broadcasted_iota(jnp.int32, (slots, lanes), 1)
    block = lax.broadcasted_iota(jnp.int32, (slots, lanes), 0) % blocks

    def add_epoch(v, e):
        at = v * 2 * total + first + e
        s_r = sh_ref[at]
        s_c = sh_ref[at + total]
        amount = lax.rem(lanes - s_c, lanes)
        moved = lane + s_c
        inside = (moved >= 0) & (moved < lanes)
        step = jnp.where(s_c >= 0, slots - 1, 1)
        edge = jnp.where(s_c >= 0, blocks - 1, 0)
        edge_ok = (block != edge) & ~inside
        for rc in range(rows // CHUNK):
            win = x_ref[e, rc * CHUNK : (rc + 1) * CHUNK]
            rolled = pltpu.roll(win, amount, axis=2)
            other = pltpu.roll(rolled, step, axis=1)
            picked = jnp.where(inside[None], rolled, jnp.where(edge_ok[None], other, 0.0))
            dest = acc_ref.at[v, pl.ds(HALO - s_r + rc * CHUNK, CHUNK)]
            dest[...] = dest[...] + picked

    def body(e, carry):
        for v in range(vels):
            add_epoch(v, e)
        return carry

    lax.fori_loop(0, epochs, body, 0, unroll=4)
    for v in range(vels):
        top_ref[v] = acc_ref[v, :HALO]
        own_ref[v] = acc_ref[v, HALO : HALO + rows]
        bottom_ref[v] = acc_ref[v, HALO + rows :]


def partial_stacks(shifts, psi, phi):
    epochs, rows, cols = psi.shape
    slots, lanes = 2 * (cols // LANES), LANES
    vels = shifts.shape[0]
    vmem = pl.BlockSpec(memory_space=pltpu.VMEM)
    spill = jax.ShapeDtypeStruct((vels, HALO, slots, lanes), jnp.float32)
    return pl.pallas_call(
        stack_kernel,
        out_shape=(jax.ShapeDtypeStruct((vels, rows, slots, lanes), jnp.float32), spill, spill),
        in_specs=[pl.BlockSpec(memory_space=pltpu.SMEM), vmem, vmem],
        out_specs=(vmem, vmem, vmem),
        scratch_shapes=[
            pltpu.VMEM((vels, rows + 2 * HALO, slots, lanes), jnp.float32),
            pltpu.VMEM((epochs, rows, slots, lanes), jnp.float32),
        ],
        cost_estimate=pl.CostEstimate(
            flops=2 * vels * epochs * rows * slots * lanes,
            bytes_accessed=4 * (epochs * rows + vels * (rows + 2 * HALO)) * slots * lanes,
            transcendentals=0,
        ),
    )(jnp.swapaxes(shifts, 1, 2).reshape(-1), psi, phi)


def per_device(psi, phi, shifts):
    epochs, rows, cols = psi.shape
    blocks = cols // LANES
    own, top, bottom = partial_stacks(shifts, psi, phi)
    count = lax.axis_size("tile")
    forward = [(i, i + 1) for i in range(count - 1)]
    backward = [(i + 1, i) for i in range(count - 1)]
    from_above = lax.ppermute(bottom, "tile", forward)
    from_below = lax.ppermute(top, "tile", backward)
    vels = own.shape[0]
    part = own.at[:, :HALO].add(from_above).at[:, rows - HALO :].add(from_below)
    part = part.reshape(vels, rows, 2, blocks, LANES).transpose(3, 0, 2, 1, 4)
    gathered = lax.all_to_all(part, "epoch", 0, 0, tiled=True)
    best = None
    for v in range(vels):
        psi_sum = gathered[0, v, 0]
        phi_sum = gathered[0, v, 1]
        for source in range(1, gathered.shape[0]):
            psi_sum = psi_sum + gathered[source, v, 0]
            phi_sum = phi_sum + gathered[source, v, 1]
        ratio = psi_sum / jnp.sqrt(phi_sum)
        best = ratio if best is None else jnp.maximum(best, ratio)
    return best


def solution(mesh):
    placed = (P("epoch", "tile", None), P("epoch", "tile", None), P())
    return jax.shard_map(
        per_device, mesh=mesh, in_specs=placed, out_specs=P("tile", "epoch"), check_vma=False
    )
```

```python
import jax
import jax.numpy as jnp
from jax import lax
from jax.experimental import pallas as pl
from jax.experimental.pallas import tpu as pltpu
from jax.sharding import PartitionSpec as P

HALO = 16
LANES = 128
CHUNK = 16


def stack_kernel(sh_ref, psi_ref, phi_ref, own_ref, top_ref, bottom_ref, acc_ref, x_ref):
    epochs, rows, slots, lanes = x_ref.shape
    blocks = slots // 2

    def pack(e, carry):
        for a in range(rows // CHUNK):
            here = slice(a * CHUNK, (a + 1) * CHUNK)
            pieces = [
                src[e, here, j * lanes : (j + 1) * lanes]
                for src in (psi_ref, phi_ref)
                for j in range(blocks)
            ]
            x_ref[e, here] = jnp.swapaxes(jnp.stack(pieces, axis=0), 0, 1)
        return carry

    lax.fori_loop(0, epochs, pack, 0)
    vels = acc_ref.shape[0]
    total = sh_ref.shape[0] // (2 * vels)
    first = lax.axis_index("epoch") * epochs

    acc_ref[...] = jnp.zeros(acc_ref.shape, jnp.float32)
    lane = lax.broadcasted_iota(jnp.int32, (slots, lanes), 1)
    block = lax.broadcasted_iota(jnp.int32, (slots, lanes), 0) % blocks

    def add_epoch(v, e):
        at = v * 2 * total + first + e
        s_r = sh_ref[at]
        s_c = sh_ref[at + total]
        amount = lax.rem(lanes - s_c, lanes)
        moved = lane + s_c
        inside = (moved >= 0) & (moved < lanes)
        step = jnp.where(s_c >= 0, slots - 1, 1)
        edge = jnp.where(s_c >= 0, blocks - 1, 0)
        edge_ok = (block != edge) & ~inside
        for rc in range(rows // CHUNK):
            win = x_ref[e, rc * CHUNK : (rc + 1) * CHUNK]
            rolled = pltpu.roll(win, amount, axis=2)
            other = pltpu.roll(rolled, step, axis=1)
            picked = jnp.where(inside[None], rolled, jnp.where(edge_ok[None], other, 0.0))
            dest = acc_ref.at[v, pl.ds(HALO - s_r + rc * CHUNK, CHUNK)]
            dest[...] = dest[...] + picked

    def body(e, carry):
        for v in range(vels):
            add_epoch(v, e)
        return carry

    lax.fori_loop(0, epochs, body, 0, unroll=4)
    for v in range(vels):
        top_ref[v] = acc_ref[v, :HALO]
        own_ref[v] = acc_ref[v, HALO : HALO + rows]
        bottom_ref[v] = acc_ref[v, HALO + rows :]


def partial_stacks(shifts, psi, phi):
    epochs, rows, cols = psi.shape
    slots, lanes = 2 * (cols // LANES), LANES
    vels = shifts.shape[0]
    vmem = pl.BlockSpec(memory_space=pltpu.VMEM)
    spill = jax.ShapeDtypeStruct((vels, HALO, slots, lanes), jnp.float32)
    return pl.pallas_call(
        stack_kernel,
        out_shape=(jax.ShapeDtypeStruct((vels, rows, slots, lanes), jnp.float32), spill, spill),
        in_specs=[pl.BlockSpec(memory_space=pltpu.SMEM), vmem, vmem],
        out_specs=(vmem, vmem, vmem),
        scratch_shapes=[
            pltpu.VMEM((vels, rows + 2 * HALO, slots, lanes), jnp.float32),
            pltpu.VMEM((epochs, rows, slots, lanes), jnp.float32),
        ],
        cost_estimate=pl.CostEstimate(
            flops=2 * vels * epochs * rows * slots * lanes,
            bytes_accessed=4 * (epochs * rows + vels * (rows + 2 * HALO)) * slots * lanes,
            transcendentals=0,
        ),
    )(jnp.swapaxes(shifts, 1, 2).reshape(-1), psi, phi)


def per_device(psi, phi, shifts):
    epochs, rows, cols = psi.shape
    blocks = cols // LANES
    own, top, bottom = partial_stacks(shifts, psi, phi)
    count = lax.axis_size("tile")
    forward = [(i, i + 1) for i in range(count - 1)]
    backward = [(i + 1, i) for i in range(count - 1)]
    from_above = lax.ppermute(bottom, "tile", forward)
    from_below = lax.ppermute(top, "tile", backward)
    vels = own.shape[0]
    middle = jnp.zeros((vels, rows - 2 * HALO) + own.shape[2:], jnp.float32)
    part = own + jnp.concatenate([from_above, middle, from_below], axis=1)
    part = part.reshape(vels, rows, 2, blocks, LANES).transpose(3, 0, 2, 1, 4)
    gathered = lax.all_to_all(part, "epoch", 0, 0, tiled=True)
    best = None
    for v in range(vels):
        psi_sum = gathered[0, v, 0]
        phi_sum = gathered[0, v, 1]
        for source in range(1, gathered.shape[0]):
            psi_sum = psi_sum + gathered[source, v, 0]
            phi_sum = phi_sum + gathered[source, v, 1]
        ratio = psi_sum / jnp.sqrt(phi_sum)
        best = ratio if best is None else jnp.maximum(best, ratio)
    return best


def solution(mesh):
    placed = (P("epoch", "tile", None), P("epoch", "tile", None), P())
    return jax.shard_map(
        per_device, mesh=mesh, in_specs=placed, out_specs=P("tile", "epoch"), check_vma=False
    )
```

```python
import jax
import jax.numpy as jnp
from jax import lax
from jax.experimental import pallas as pl
from jax.experimental.pallas import tpu as pltpu
from jax.sharding import PartitionSpec as P

HALO = 16
LANES = 128
CHUNK = 8


def stack_kernel(sh_ref, psi_ref, phi_ref, own_ref, top_ref, bottom_ref, acc_ref, x_ref):
    epochs, rows, slots, lanes = x_ref.shape
    blocks = slots // 2

    def pack(e, carry):
        for a in range(rows // CHUNK):
            here = slice(a * CHUNK, (a + 1) * CHUNK)
            pieces = [
                src[e, here, j * lanes : (j + 1) * lanes]
                for src in (psi_ref, phi_ref)
                for j in range(blocks)
            ]
            x_ref[e, here] = jnp.swapaxes(jnp.stack(pieces, axis=0), 0, 1)
        return carry

    lax.fori_loop(0, epochs, pack, 0)
    vels = acc_ref.shape[0]
    total = sh_ref.shape[0] // (2 * vels)
    first = lax.axis_index("epoch") * epochs

    acc_ref[...] = jnp.zeros(acc_ref.shape, jnp.float32)
    lane = lax.broadcasted_iota(jnp.int32, (slots, lanes), 1)
    block = lax.broadcasted_iota(jnp.int32, (slots, lanes), 0) % blocks

    def add_epoch(v, e):
        at = v * 2 * total + first + e
        s_r = sh_ref[at]
        s_c = sh_ref[at + total]
        amount = lax.rem(lanes - s_c, lanes)
        moved = lane + s_c
        inside = (moved >= 0) & (moved < lanes)
        step = jnp.where(s_c >= 0, slots - 1, 1)
        edge = jnp.where(s_c >= 0, blocks - 1, 0)
        edge_ok = (block != edge) & ~inside
        for rc in range(rows // CHUNK):
            win = x_ref[e, rc * CHUNK : (rc + 1) * CHUNK]
            rolled = pltpu.roll(win, amount, axis=2)
            other = pltpu.roll(rolled, step, axis=1)
            picked = jnp.where(inside[None], rolled, jnp.where(edge_ok[None], other, 0.0))
            dest = acc_ref.at[v, pl.ds(HALO - s_r + rc * CHUNK, CHUNK)]
            dest[...] = dest[...] + picked

    def body(e, carry):
        for v in range(vels):
            add_epoch(v, e)
        return carry

    lax.fori_loop(0, epochs, body, 0, unroll=True)
    for v in range(vels):
        top_ref[v] = acc_ref[v, :HALO]
        own_ref[v] = acc_ref[v, HALO : HALO + rows]
        bottom_ref[v] = acc_ref[v, HALO + rows :]


def partial_stacks(shifts, psi, phi):
    epochs, rows, cols = psi.shape
    slots, lanes = 2 * (cols // LANES), LANES
    vels = shifts.shape[0]
    vmem = pl.BlockSpec(memory_space=pltpu.VMEM)
    spill = jax.ShapeDtypeStruct((vels, HALO, slots, lanes), jnp.float32)
    return pl.pallas_call(
        stack_kernel,
        out_shape=(jax.ShapeDtypeStruct((vels, rows, slots, lanes), jnp.float32), spill, spill),
        in_specs=[pl.BlockSpec(memory_space=pltpu.SMEM), vmem, vmem],
        out_specs=(vmem, vmem, vmem),
        scratch_shapes=[
            pltpu.VMEM((vels, rows + 2 * HALO, slots, lanes), jnp.float32),
            pltpu.VMEM((epochs, rows, slots, lanes), jnp.float32),
        ],
        cost_estimate=pl.CostEstimate(
            flops=2 * vels * epochs * rows * slots * lanes,
            bytes_accessed=4 * (epochs * rows + vels * (rows + 2 * HALO)) * slots * lanes,
            transcendentals=0,
        ),
    )(jnp.swapaxes(shifts, 1, 2).reshape(-1), psi, phi)


def per_device(psi, phi, shifts):
    epochs, rows, cols = psi.shape
    blocks = cols // LANES
    own, top, bottom = partial_stacks(shifts, psi, phi)
    count = lax.axis_size("tile")
    forward = [(i, i + 1) for i in range(count - 1)]
    backward = [(i + 1, i) for i in range(count - 1)]
    from_above = lax.ppermute(bottom, "tile", forward)
    from_below = lax.ppermute(top, "tile", backward)
    vels = own.shape[0]
    middle = jnp.zeros((vels, rows - 2 * HALO) + own.shape[2:], jnp.float32)
    part = own + jnp.concatenate([from_above, middle, from_below], axis=1)
    part = part.reshape(vels, rows, 2, blocks, LANES).transpose(3, 0, 2, 1, 4)
    gathered = lax.all_to_all(part, "epoch", 0, 0, tiled=True)
    best = None
    for v in range(vels):
        psi_sum = gathered[0, v, 0]
        phi_sum = gathered[0, v, 1]
        for source in range(1, gathered.shape[0]):
            psi_sum = psi_sum + gathered[source, v, 0]
            phi_sum = phi_sum + gathered[source, v, 1]
        ratio = psi_sum / jnp.sqrt(phi_sum)
        best = ratio if best is None else jnp.maximum(best, ratio)
    return best


def solution(mesh):
    placed = (P("epoch", "tile", None), P("epoch", "tile", None), P())
    return jax.shard_map(
        per_device, mesh=mesh, in_specs=placed, out_specs=P("tile", "epoch"), check_vma=False
    )
```

```python
import jax
import jax.numpy as jnp
from jax import lax
from jax.experimental import pallas as pl
from jax.experimental.pallas import tpu as pltpu
from jax.sharding import PartitionSpec as P

HALO = 16
LANES = 128
CHUNK = 8


def stack_kernel(sh_ref, psi_ref, phi_ref, own_ref, top_ref, bottom_ref, acc_ref, x_ref):
    epochs, rows, slots, lanes = x_ref.shape
    blocks = slots // 2

    def pack(e, carry):
        for a in range(rows // CHUNK):
            here = slice(a * CHUNK, (a + 1) * CHUNK)
            pieces = [
                src[e, here, j * lanes : (j + 1) * lanes]
                for src in (psi_ref, phi_ref)
                for j in range(blocks)
            ]
            x_ref[e, here] = jnp.swapaxes(jnp.stack(pieces, axis=0), 0, 1)
        return carry

    lax.fori_loop(0, epochs, pack, 0, unroll=True)
    vels = acc_ref.shape[0]
    total = sh_ref.shape[0] // (2 * vels)
    first = lax.axis_index("epoch") * epochs

    acc_ref[...] = jnp.zeros(acc_ref.shape, jnp.float32)
    lane = lax.broadcasted_iota(jnp.int32, (slots, lanes), 1)
    block = lax.broadcasted_iota(jnp.int32, (slots, lanes), 0) % blocks

    def add_epoch(v, e):
        at = v * 2 * total + first + e
        s_r = sh_ref[at]
        s_c = sh_ref[at + total]
        amount = lax.rem(lanes - s_c, lanes)
        moved = lane + s_c
        inside = (moved >= 0) & (moved < lanes)
        step = jnp.where(s_c >= 0, slots - 1, 1)
        edge = jnp.where(s_c >= 0, blocks - 1, 0)
        edge_ok = (block != edge) & ~inside
        for rc in range(rows // CHUNK):
            win = x_ref[e, rc * CHUNK : (rc + 1) * CHUNK]
            rolled = pltpu.roll(win, amount, axis=2)
            other = pltpu.roll(rolled, step, axis=1)
            picked = jnp.where(inside[None], rolled, jnp.where(edge_ok[None], other, 0.0))
            dest = acc_ref.at[v, pl.ds(HALO - s_r + rc * CHUNK, CHUNK)]
            dest[...] = dest[...] + picked

    def body(e, carry):
        for v in range(vels):
            add_epoch(v, e)
        return carry

    lax.fori_loop(0, epochs, body, 0, unroll=True)
    for v in range(vels):
        top_ref[v] = acc_ref[v, :HALO]
        own_ref[v] = acc_ref[v, HALO : HALO + rows]
        bottom_ref[v] = acc_ref[v, HALO + rows :]


def partial_stacks(shifts, psi, phi):
    epochs, rows, cols = psi.shape
    slots, lanes = 2 * (cols // LANES), LANES
    vels = shifts.shape[0]
    vmem = pl.BlockSpec(memory_space=pltpu.VMEM)
    spill = jax.ShapeDtypeStruct((vels, HALO, slots, lanes), jnp.float32)
    return pl.pallas_call(
        stack_kernel,
        out_shape=(jax.ShapeDtypeStruct((vels, rows, slots, lanes), jnp.float32), spill, spill),
        in_specs=[pl.BlockSpec(memory_space=pltpu.SMEM), vmem, vmem],
        out_specs=(vmem, vmem, vmem),
        scratch_shapes=[
            pltpu.VMEM((vels, rows + 2 * HALO, slots, lanes), jnp.float32),
            pltpu.VMEM((epochs, rows, slots, lanes), jnp.float32),
        ],
        cost_estimate=pl.CostEstimate(
            flops=2 * vels * epochs * rows * slots * lanes,
            bytes_accessed=4 * (epochs * rows + vels * (rows + 2 * HALO)) * slots * lanes,
            transcendentals=0,
        ),
    )(jnp.swapaxes(shifts, 1, 2).reshape(-1), psi, phi)


def per_device(psi, phi, shifts):
    epochs, rows, cols = psi.shape
    blocks = cols // LANES
    own, top, bottom = partial_stacks(shifts, psi, phi)
    count = lax.axis_size("tile")
    forward = [(i, i + 1) for i in range(count - 1)]
    backward = [(i + 1, i) for i in range(count - 1)]
    from_above = lax.ppermute(bottom, "tile", forward)
    from_below = lax.ppermute(top, "tile", backward)
    vels = own.shape[0]
    middle = jnp.zeros((vels, rows - 2 * HALO) + own.shape[2:], jnp.float32)
    part = own + jnp.concatenate([from_above, middle, from_below], axis=1)
    part = part.reshape(vels, rows, 2, blocks, LANES).transpose(3, 0, 2, 1, 4)
    gathered = lax.all_to_all(part, "epoch", 0, 0, tiled=True)
    best = None
    for v in range(vels):
        psi_sum = gathered[0, v, 0]
        phi_sum = gathered[0, v, 1]
        for source in range(1, gathered.shape[0]):
            psi_sum = psi_sum + gathered[source, v, 0]
            phi_sum = phi_sum + gathered[source, v, 1]
        ratio = psi_sum / jnp.sqrt(phi_sum)
        best = ratio if best is None else jnp.maximum(best, ratio)
    return best


def solution(mesh):
    placed = (P("epoch", "tile", None), P("epoch", "tile", None), P())
    return jax.shard_map(
        per_device, mesh=mesh, in_specs=placed, out_specs=P("tile", "epoch"), check_vma=False
    )
```
